512 devices in a mesh: head: 8 (over z), ctx: 64 (over x, y, core).
Axes of the slice: x: 4, y: 8, z: 8, core: 2. Of those that a mesh axis runs over, the one named last changes fastest.
Arguments:
- query_bits: int32 [256, 16384], P('head', 'ctx'), may hold values from 0 to 65535
- key_bits: int32 [256, 16384], P('head', 'ctx'), may hold values from 0 to 65535
- values: bfloat16 [16384, 4096], P('ctx', 'head'), may hold values from -6 to 6
- grad_out: bfloat16 [64, 256, 4096], P('ctx', 'head'), may hold values from -6 to 6
- tile_mask: int32 [64, 2, 2], P('ctx'), may hold values 0 or 1
Outputs:
- query_grad: bfloat16 [16384, 4096], P('ctx', 'head')
- key_grad: bfloat16 [16384, 4096], P('ctx', 'head')
- value_grad: bfloat16 [16384, 4096], P('ctx', 'head')
The draws below stay inside these ranges and needn't reach their ends.
All inputs are finite; a program needn't handle non-finite values. No bound on the sum of `tile_mask` on one device may be relied on, other than what follows from the above.
Results may differ from the reference program's by a relative error of at most 0.0049.
Values may be sent and summed in bfloat16 or wider, within the bound.
No kernel may reach another device: no remote copies, remote signals or barrier semaphores. Data moves between devices by JAX's collectives and lax.ppermute only.
A program may use at most 128 MiB of HBM per device.

```python
import math
import jax
import jax.numpy as jnp
from jax import lax

HEADS = 32
HD = 128
TILE = 128
TOK_DEV = 256
D = 4096
WORDS = 8
TB = 2
STRETCHES = 64
TOKENS = 16384


def set_ends(result, key, smallest, high):
    index_at = [jax.random.randint(jax.random.fold_in(key, axis), (), 0, length) for axis, length in enumerate(result.shape)]
    widest = result.shape.index(max(result.shape))
    beside = index_at[:widest] + [(index_at[widest] + 1) % result.shape[widest]] + index_at[widest + 1:]
    return result.at[tuple(index_at)].set(smallest).at[tuple(beside)].set(high)


def block_levels(rng, shape, split, least, high):
    factor_of = 1.0
    for dim, shards_of in split:
        steps = jax.random.uniform(jax.random.fold_in(jax.random.fold_in(rng, 6), dim), (shards_of,), jnp.float32, least / len(split), high / len(split))
        factor_of = factor_of * jnp.repeat(jnp.exp(steps), shape[dim] // shards_of).reshape((-1,) + (1,) * (len(shape) - 1 - dim))
    return factor_of


def scatter_about(key, dims, width, limit, pieces=(), kind=jnp.bfloat16):
    drawn = jax.random.normal(key, dims, jnp.float32) * width
    if len(pieces) > 0:
        drawn = block_levels(key, dims, pieces, -0.22, 0.18) * drawn
    return jnp.clip(drawn, min=-limit, max=limit).astype(kind)


def setup_inputs(seed: int = 0) -> dict:
    key_of = jax.random.split(jax.random.key(seed), 6)
    query_bits = set_ends(jax.random.randint(key_of[0], (HEADS * WORDS, TOKENS), 0, 65536), jax.random.fold_in(key_of[0], 1), 0, 65535).astype(jnp.int32)
    key_bits = set_ends(jax.random.randint(key_of[1], (HEADS * WORDS, TOKENS), 0, 65536), jax.random.fold_in(key_of[1], 1), 0, 65535).astype(jnp.int32)
    values = scatter_about(key_of[2], (TOKENS, D), 1.0, 6.0, ((0, 64), (1, 8)))
    grad_out = scatter_about(key_of[3], (STRETCHES, TOK_DEV, D), 1.0, 6.0, ((0, 64), (1, 8)))
    tile_mask = set_ends((jax.random.randint(key_of[4], (STRETCHES, TB, TB), 0, 2) < 1).astype(jnp.int32), jax.random.fold_in(key_of[4], 1), 0, 1)
    return dict(query_bits=query_bits, key_bits=key_bits, values=values, grad_out=grad_out, tile_mask=tile_mask)


def unpack_bits(packed, heads_here):
    shifts = jnp.arange(16, dtype=jnp.int32).reshape(1, 1, 16, 1)
    spread = jnp.right_shift(packed.reshape(heads_here, -1, 1, packed.shape[-1]), shifts)
    return jnp.bitwise_and(spread, 1).astype(jnp.bfloat16).reshape(heads_here, -1, packed.shape[-1])

def token_mask(tiles, tile_size):
    tile_count = tiles.shape[0]
    tile_index = jnp.arange(tile_count, dtype=jnp.int32)
    lower = tile_index[:, None] > tile_index[None, :]
    diagonal = tile_index[:, None] == tile_index[None, :]
    allowed = jnp.where(diagonal, 1.0, jnp.where(lower, tiles.astype(jnp.float32), 0.0)).astype(jnp.float32)
    span_width = tile_count * tile_size
    expanded = jnp.broadcast_to(allowed[:, None, :, None], (tile_count, tile_size, tile_count, tile_size)).reshape(span_width, span_width)
    position = jnp.arange(span_width, dtype=jnp.int32)
    return jnp.where(position[:, None] >= position[None, :], expanded, 0.0).astype(jnp.float32)

def stretch_grads(query_spk, key_spk, value_rows, grad_rows, state, adjoint, keep_mask, att_scale):
    pair_dots = jnp.dot(grad_rows, value_rows.T, preferred_element_type=jnp.float32)
    grad_weights = (att_scale * pair_dots * keep_mask).astype(jnp.bfloat16)
    spike_dots = jnp.dot(query_spk.T, key_spk, preferred_element_type=jnp.float32)
    att_weights = (att_scale * spike_dots * keep_mask).astype(jnp.bfloat16)
    query_grad = jnp.dot(grad_weights, key_spk.T, preferred_element_type=jnp.float32) + att_scale * jnp.dot(grad_rows, state.T, preferred_element_type=jnp.float32)
    key_grad = jnp.dot(grad_weights.T, query_spk.T, preferred_element_type=jnp.float32) + att_scale * jnp.dot(value_rows, adjoint.T, preferred_element_type=jnp.float32)
    value_grad = jnp.dot(att_weights.T, grad_rows, preferred_element_type=jnp.float32) + att_scale * jnp.dot(key_spk.T, adjoint, preferred_element_type=jnp.float32)
    return (query_grad.astype(jnp.bfloat16), key_grad.astype(jnp.bfloat16), value_grad.astype(jnp.bfloat16))

def reference(query_bits, key_bits, values, grad_out, tile_mask):
    att_scale = 4.0 / (HD * math.sqrt(TOKENS))
    query_all = query_bits.reshape(HEADS, WORDS, TOKENS)
    key_all = key_bits.reshape(HEADS, WORDS, TOKENS)
    value_all = values.reshape(TOKENS, HEADS, HD).transpose(1, 0, 2)
    grad_all = grad_out.reshape(TOKENS, HEADS, HD).transpose(1, 0, 2)

    def one_head(head_item):
        query_words, key_words, value_head, grad_head = head_item
        query_spk = unpack_bits(query_words, 1)[0].reshape(HD, STRETCHES, TOK_DEV).transpose(1, 0, 2)
        key_spk = unpack_bits(key_words, 1)[0].reshape(HD, STRETCHES, TOK_DEV).transpose(1, 0, 2)
        value_stretches = value_head.reshape(STRETCHES, TOK_DEV, HD)
        grad_stretches = grad_head.reshape(STRETCHES, TOK_DEV, HD)
        state_terms = jnp.einsum('cdt,cte->cde', key_spk.astype(jnp.float32), value_stretches.astype(jnp.float32))
        adjoint_terms = jnp.einsum('cdt,cte->cde', query_spk.astype(jnp.float32), grad_stretches.astype(jnp.float32))
        zero_block = jnp.zeros((1, HD, HD), jnp.float32)
        states = jnp.concatenate([zero_block, jnp.cumsum(state_terms, axis=0)[:-1]], axis=0).astype(jnp.bfloat16)
        adjoints = jnp.concatenate([jnp.cumsum(adjoint_terms[::-1], axis=0)[::-1][1:], zero_block], axis=0).astype(jnp.bfloat16)

        def one_stretch(stretch_item):
            stretch_query, stretch_key, stretch_value, stretch_grad, stretch_state, stretch_adjoint, stretch_tiles = stretch_item
            return stretch_grads(stretch_query, stretch_key, stretch_value, stretch_grad, stretch_state, stretch_adjoint, token_mask(stretch_tiles, TILE), att_scale)
        grads_query, grads_key, grads_value = lax.map(one_stretch, (query_spk, key_spk, value_stretches, grad_stretches, states, adjoints, tile_mask))
        return (grads_query.reshape(TOKENS, HD), grads_key.reshape(TOKENS, HD), grads_value.reshape(TOKENS, HD))
    out_query, out_key, out_value = lax.map(one_head, (query_all, key_all, value_all, grad_all))
    return (out_query.transpose(1, 0, 2).reshape(TOKENS, HEADS * HD), out_key.transpose(1, 0, 2).reshape(TOKENS, HEADS * HD), out_value.transpose(1, 0, 2).reshape(TOKENS, HEADS * HD))
```

```python
import math

import jax
import jax.numpy as jnp
import numpy as np
from jax import lax
from jax.sharding import Mesh
from jax.sharding import PartitionSpec as P

HD = 128
CTX = ("x", "y", "core")


def unpack_bits(packed, heads_here):
    shifts = jnp.arange(16, dtype=jnp.int32).reshape(1, 1, 16, 1)
    spread = jnp.right_shift(packed.reshape(heads_here, -1, 1, packed.shape[-1]), shifts)
    return jnp.bitwise_and(spread, 1).astype(jnp.bfloat16).reshape(heads_here, -1, packed.shape[-1])


def token_mask(tiles, tile_size):
    tile_count = tiles.shape[0]
    tile_index = jnp.arange(tile_count, dtype=jnp.int32)
    lower = tile_index[:, None] > tile_index[None, :]
    diagonal = tile_index[:, None] == tile_index[None, :]
    allowed = jnp.where(diagonal, 1.0, jnp.where(lower, tiles.astype(jnp.float32), 0.0))
    span_width = tile_count * tile_size
    expanded = jnp.broadcast_to(
        allowed[:, None, :, None], (tile_count, tile_size, tile_count, tile_size)
    ).reshape(span_width, span_width)
    position = jnp.arange(span_width, dtype=jnp.int32)
    return jnp.where(position[:, None] >= position[None, :], expanded, 0.0)


def swap_core(a):
    return lax.ppermute(a, "core", [(0, 1), (1, 0)])


def gather_heads(grad_out, n_head, width):
    me = lax.axis_index("head")
    tok_part = grad_out.shape[1]
    blocks = grad_out[0].reshape(tok_part, n_head, width).transpose(1, 0, 2)
    recv = [lax.dynamic_index_in_dim(blocks, me, 0, keepdims=False)]
    for k in range(1, n_head):
        dst = lax.rem(me + k, n_head)
        piece = lax.dynamic_index_in_dim(blocks, dst, 0, keepdims=False)
        recv.append(lax.ppermute(piece, "head", [(i, (i + k) % n_head) for i in range(n_head)]))
    stacked = jnp.stack(recv)
    order = lax.rem(me - jnp.arange(n_head, dtype=jnp.int32) + n_head, n_head)
    return jnp.take(stacked, order, axis=0).reshape(n_head * tok_part, width)


def masked_sum(stack, keep):
    return jnp.sum(jnp.where(keep.reshape((-1,) + (1,) * (stack.ndim - 1)), stack, 0.0), axis=0)


def carried_sums(state_term, adj_term, sizes):
    n_x, n_y, _ = sizes
    me_core = lax.axis_index("core")
    me_y = lax.axis_index("y")
    me_x = lax.axis_index("x")
    heads = state_term.shape[0]
    half = heads // 2
    terms = jnp.stack([state_term, adj_term])
    other = swap_core(terms)
    chip = terms + other
    in_chip_s = jnp.where(me_core == 1, other[0], 0.0)
    in_chip_a = jnp.where(me_core == 0, other[1], 0.0)
    mine = lax.dynamic_slice_in_dim(chip, me_core * half, half, axis=1)
    row = lax.all_gather(mine, "y")
    y_index = jnp.arange(n_y, dtype=jnp.int32)
    pre_y = masked_sum(row[:, 0], y_index < me_y)
    suf_y = masked_sum(row[:, 1], y_index > me_y)
    total = jnp.sum(row, axis=0)
    cols = lax.all_gather(total, "x")
    x_index = jnp.arange(n_x, dtype=jnp.int32)
    pre_x = masked_sum(cols[:, 0], x_index < me_x)
    suf_x = masked_sum(cols[:, 1], x_index > me_x)
    part = jnp.stack([pre_x + pre_y, suf_x + suf_y])
    part_other = swap_core(part)
    full = jnp.where(
        me_core == 0,
        jnp.concatenate([part, part_other], axis=1),
        jnp.concatenate([part_other, part], axis=1),
    )
    return full[0] + in_chip_s, full[1] + in_chip_a


def make_local(sizes, n_head):
    n_ctx = sizes[0] * sizes[1] * sizes[2]

    def local(query_bits, key_bits, values, grad_out, tile_mask):
        f32 = jnp.float32
        bf16 = jnp.bfloat16
        tok_rows = values.shape[0]
        head_group = values.shape[1] // HD
        att_scale = 4.0 / (HD * math.sqrt(tok_rows * n_ctx))
        q = unpack_bits(query_bits, head_group)
        k = unpack_bits(key_bits, head_group)
        v = values.reshape(tok_rows, head_group, HD)
        g = gather_heads(grad_out, n_head, values.shape[1]).reshape(tok_rows, head_group, HD)
        state_term = jnp.einsum("hds,she->hde", k, v, preferred_element_type=f32)
        adj_term = jnp.einsum("hdt,the->hde", q, g, preferred_element_type=f32)
        state_sum, adj_sum = carried_sums(state_term, adj_term, sizes)
        state = state_sum.astype(bf16)
        adjoint = adj_sum.astype(bf16)

        keep = token_mask(tile_mask[0], tok_rows // tile_mask.shape[1])
        pair = jnp.einsum("the,she->hts", g, v, preferred_element_type=f32)
        grad_w = (att_scale * pair * keep).astype(bf16)
        spk = jnp.einsum("hdt,hds->hts", q, k, preferred_element_type=f32)
        att_w = (att_scale * spk * keep).astype(bf16)
        query_grad = jnp.einsum("hts,hds->thd", grad_w, k, preferred_element_type=f32) + att_scale * jnp.einsum(
            "the,hde->thd", g, state, preferred_element_type=f32
        )
        key_grad = jnp.einsum("hts,hdt->shd", grad_w, q, preferred_element_type=f32) + att_scale * jnp.einsum(
            "she,hde->shd", v, adjoint, preferred_element_type=f32
        )
        value_grad = jnp.einsum("hts,the->she", att_w, g, preferred_element_type=f32) + att_scale * jnp.einsum(
            "hds,hde->she", k, adjoint, preferred_element_type=f32
        )
        shape = (tok_rows, head_group * HD)
        return (
            query_grad.astype(bf16).reshape(shape),
            key_grad.astype(bf16).reshape(shape),
            value_grad.astype(bf16).reshape(shape),
        )

    return local


def ctx_sizes(devices):
    n_ctx = devices.shape[1]
    n_core = 2
    try:
        n_y = len({d.coords[1] for d in devices[0]})
    except Exception:
        n_y = 8
    if n_y <= 0 or n_ctx % (n_core * n_y) != 0:
        n_y = 8
    return (n_ctx // (n_core * n_y), n_y, n_core)


def solution(mesh):
    devices = np.asarray(mesh.devices)
    sizes = ctx_sizes(devices)
    n_head = devices.shape[0]
    fine = Mesh(devices.reshape((n_head,) + sizes), ("head",) + CTX)
    return jax.shard_map(
        make_local(sizes, n_head),
        mesh=fine,
        in_specs=(
            P("head", CTX),
            P("head", CTX),
            P(CTX, "head"),
            P(CTX, "head", None),
            P(CTX, None, None),
        ),
        out_specs=(P(CTX, "head"), P(CTX, "head"), P(CTX, "head")),
        check_vma=False,
    )
```

```python
import math

import jax
import jax.numpy as jnp
import numpy as np
from jax import lax
from jax.sharding import Mesh
from jax.sharding import PartitionSpec as P

HD = 128
CTX = ("x", "y", "core")

def unpack_bits(packed, heads_here):
    shifts = jnp.arange(16, dtype=jnp.int32).reshape(1, 1, 16, 1)
    spread = jnp.right_shift(packed.reshape(heads_here, -1, 1, packed.shape[-1]), shifts)
    return jnp.bitwise_and(spread, 1).astype(jnp.bfloat16).reshape(heads_here, -1, packed.shape[-1])


def token_mask(tiles, tile_size):
    tile_count = tiles.shape[0]
    tile_index = jnp.arange(tile_count, dtype=jnp.int32)
    lower = tile_index[:, None] > tile_index[None, :]
    diagonal = tile_index[:, None] == tile_index[None, :]
    allowed = jnp.where(diagonal, 1.0, jnp.where(lower, tiles.astype(jnp.float32), 0.0))
    span_width = tile_count * tile_size
    expanded = jnp.broadcast_to(
        allowed[:, None, :, None], (tile_count, tile_size, tile_count, tile_size)
    ).reshape(span_width, span_width)
    position = jnp.arange(span_width, dtype=jnp.int32)
    return jnp.where(position[:, None] >= position[None, :], expanded, 0.0)


def gather_heads(grad_out, n_head, width):
    tok_part = grad_out.shape[1]
    blocks = grad_out[0].reshape(tok_part, n_head, width).transpose(1, 0, 2)
    got = lax.all_to_all(blocks, "head", 0, 0, tiled=True)
    return got.reshape(n_head * tok_part, width)


def carried_sums(state_term, adj_term, n_ctx):
    f32 = jnp.float32
    heads = state_term.shape[0]
    terms = jnp.concatenate([state_term, adj_term], axis=0).reshape(n_ctx, -1, HD)
    got = lax.all_to_all(terms, CTX, 0, 0, tiled=True)
    me = lax.axis_index(CTX)
    row = jnp.arange(n_ctx, dtype=jnp.int32)[:, None]
    col = jnp.arange(n_ctx, dtype=jnp.int32)[None, :]
    mix = jnp.where(me < n_ctx // 2, col < row, col > row).astype(f32)
    sums = jnp.dot(
        mix, got.reshape(n_ctx, -1), precision=lax.Precision.HIGHEST, preferred_element_type=f32
    )
    back = lax.all_to_all(sums.astype(jnp.bfloat16).reshape(n_ctx, -1, HD), CTX, 0, 0, tiled=True)
    both = back.reshape(2, heads, HD, HD)
    return both[0], both[1]


def make_local(sizes, n_head):
    n_ctx = sizes[0] * sizes[1] * sizes[2]

    def local(query_bits, key_bits, values, grad_out, tile_mask):
        f32 = jnp.float32
        bf16 = jnp.bfloat16
        tok_rows = values.shape[0]
        head_group = values.shape[1] // HD
        att_scale = 4.0 / (HD * math.sqrt(tok_rows * n_ctx))
        q = unpack_bits(query_bits, head_group)
        k = unpack_bits(key_bits, head_group)
        v = values.reshape(tok_rows, head_group, HD)
        g = gather_heads(grad_out, n_head, values.shape[1]).reshape(tok_rows, head_group, HD)
        state_term = jnp.einsum("hds,she->hde", k, v, preferred_element_type=f32)
        adj_term = jnp.einsum("hdt,the->hde", q, g, preferred_element_type=f32)
        state, adjoint = carried_sums(state_term, adj_term, n_ctx)

        keep = token_mask(tile_mask[0], tok_rows // tile_mask.shape[1])
        pair = jnp.einsum("the,she->hts", g, v, preferred_element_type=f32)
        grad_w = (att_scale * pair * keep).astype(bf16)
        spk = jnp.einsum("hdt,hds->hts", q, k, preferred_element_type=f32)
        att_w = (att_scale * spk * keep).astype(bf16)
        query_grad = jnp.einsum("hts,hds->thd", grad_w, k, preferred_element_type=f32) + att_scale * jnp.einsum(
            "the,hde->thd", g, state, preferred_element_type=f32
        )
        key_grad = jnp.einsum("hts,hdt->shd", grad_w, q, preferred_element_type=f32) + att_scale * jnp.einsum(
            "she,hde->shd", v, adjoint, preferred_element_type=f32
        )
        value_grad = jnp.einsum("hts,the->she", att_w, g, preferred_element_type=f32) + att_scale * jnp.einsum(
            "hds,hde->she", k, adjoint, preferred_element_type=f32
        )
        shape = (tok_rows, head_group * HD)
        return (
            query_grad.astype(bf16).reshape(shape),
            key_grad.astype(bf16).reshape(shape),
            value_grad.astype(bf16).reshape(shape),
        )

    return local


def ctx_sizes(devices):
    n_ctx = devices.shape[1]
    n_core = 2
    try:
        n_y = len({d.coords[1] for d in devices[0]})
    except Exception:
        n_y = 8
    if n_y <= 0 or n_ctx % (n_core * n_y) != 0:
        n_y = 8
    return (n_ctx // (n_core * n_y), n_y, n_core)


def solution(mesh):
    devices = np.asarray(mesh.devices)
    sizes = ctx_sizes(devices)
    n_head = devices.shape[0]
    fine = Mesh(devices.reshape((n_head,) + sizes), ("head",) + CTX)
    return jax.shard_map(
        make_local(sizes, n_head),
        mesh=fine,
        in_specs=(
            P("head", CTX),
            P("head", CTX),
            P(CTX, "head"),
            P(CTX, "head", None),
            P(CTX, None, None),
        ),
        out_specs=(P(CTX, "head"), P(CTX, "head"), P(CTX, "head")),
        check_vma=False,
    )
```

```python
import math

import jax
import jax.numpy as jnp
import numpy as np
from jax import lax
from jax.sharding import Mesh
from jax.sharding import PartitionSpec as P

HD = 128
CTX = ("x", "y", "core")
CHIPS = ("x", "y")

def unpack_bits(packed, heads_here):
    shifts = jnp.arange(16, dtype=jnp.int32).reshape(1, 1, 16, 1)
    spread = jnp.right_shift(packed.reshape(heads_here, -1, 1, packed.shape[-1]), shifts)
    return jnp.bitwise_and(spread, 1).astype(jnp.bfloat16).reshape(heads_here, -1, packed.shape[-1])


def token_mask(tiles, tile_size):
    tile_count = tiles.shape[0]
    tile_index = jnp.arange(tile_count, dtype=jnp.int32)
    lower = tile_index[:, None] > tile_index[None, :]
    diagonal = tile_index[:, None] == tile_index[None, :]
    allowed = jnp.where(diagonal, 1.0, jnp.where(lower, tiles.astype(jnp.float32), 0.0))
    span_width = tile_count * tile_size
    expanded = jnp.broadcast_to(
        allowed[:, None, :, None], (tile_count, tile_size, tile_count, tile_size)
    ).reshape(span_width, span_width)
    position = jnp.arange(span_width, dtype=jnp.int32)
    return jnp.where(position[:, None] >= position[None, :], expanded, 0.0)


def gather_heads(grad_out, n_head, width):
    tok_part = grad_out.shape[1]
    blocks = grad_out[0].reshape(tok_part, n_head, width).transpose(1, 0, 2)
    got = lax.all_to_all(blocks, "head", 0, 0, tiled=True)
    return got.reshape(n_head * tok_part, width)


def swap_core(a):
    return lax.ppermute(a, "core", [(0, 1), (1, 0)])


def carried_sums(state_term, adj_term, n_chip):
    f32 = jnp.float32
    heads = state_term.shape[0]
    core = lax.axis_index("core")
    other_s = swap_core(state_term)
    other_a = swap_core(adj_term)
    chip = jnp.stack([state_term + other_s, adj_term + other_a]).reshape(2, n_chip, -1, HD)
    mine = lax.dynamic_index_in_dim(chip, core, 0, keepdims=False)
    got = lax.all_to_all(mine, CHIPS, 0, 0, tiled=True)
    row = jnp.arange(n_chip, dtype=jnp.int32)[:, None]
    col = jnp.arange(n_chip, dtype=jnp.int32)[None, :]
    mix = jnp.where(core == 0, col < row, col > row).astype(f32)
    sums = jnp.dot(
        mix, got.reshape(n_chip, -1), precision=lax.Precision.HIGHEST, preferred_element_type=f32
    )
    back = lax.all_to_all(sums.reshape(n_chip, -1, HD), CHIPS, 0, 0, tiled=True)
    mine_p = back.reshape(heads, HD, HD)
    other_p = swap_core(mine_p)
    state_p = jnp.where(core == 0, mine_p, other_p) + jnp.where(core == 1, other_s, 0.0)
    adj_p = jnp.where(core == 0, other_p, mine_p) + jnp.where(core == 0, other_a, 0.0)
    return state_p.astype(jnp.bfloat16), adj_p.astype(jnp.bfloat16)


def make_local(sizes, n_head):
    n_ctx = sizes[0] * sizes[1] * sizes[2]

    def local(query_bits, key_bits, values, grad_out, tile_mask):
        f32 = jnp.float32
        bf16 = jnp.bfloat16
        tok_rows = values.shape[0]
        head_group = values.shape[1] // HD
        att_scale = 4.0 / (HD * math.sqrt(tok_rows * n_ctx))
        q = unpack_bits(query_bits, head_group)
        k = unpack_bits(key_bits, head_group)
        v = values.reshape(tok_rows, head_group, HD)
        g = gather_heads(grad_out, n_head, values.shape[1]).reshape(tok_rows, head_group, HD)
        state_term = jnp.einsum("hds,she->hde", k, v, preferred_element_type=f32)
        adj_term = jnp.einsum("hdt,the->hde", q, g, preferred_element_type=f32)
        state, adjoint = carried_sums(state_term, adj_term, n_ctx // sizes[2])

        keep = token_mask(tile_mask[0], tok_rows // tile_mask.shape[1])
        pair = jnp.einsum("the,she->hts", g, v, preferred_element_type=f32)
        grad_w = (att_scale * pair * keep).astype(bf16)
        spk = jnp.einsum("hdt,hds->hts", q, k, preferred_element_type=f32)
        att_w = (att_scale * spk * keep).astype(bf16)
        query_grad = jnp.einsum("hts,hds->thd", grad_w, k, preferred_element_type=f32) + att_scale * jnp.einsum(
            "the,hde->thd", g, state, preferred_element_type=f32
        )
        key_grad = jnp.einsum("hts,hdt->shd", grad_w, q, preferred_element_type=f32) + att_scale * jnp.einsum(
            "she,hde->shd", v, adjoint, preferred_element_type=f32
        )
        value_grad = jnp.einsum("hts,the->she", att_w, g, preferred_element_type=f32) + att_scale * jnp.einsum(
            "hds,hde->she", k, adjoint, preferred_element_type=f32
        )
        shape = (tok_rows, head_group * HD)
        return (
            query_grad.astype(bf16).reshape(shape),
            key_grad.astype(bf16).reshape(shape),
            value_grad.astype(bf16).reshape(shape),
        )

    return local


def ctx_sizes(devices):
    n_ctx = devices.shape[1]
    n_core = 2
    try:
        n_y = len({d.coords[1] for d in devices[0]})
    except Exception:
        n_y = 8
    if n_y <= 0 or n_ctx % (n_core * n_y) != 0:
        n_y = 8
    return (n_ctx // (n_core * n_y), n_y, n_core)


def solution(mesh):
    devices = np.asarray(mesh.devices)
    sizes = ctx_sizes(devices)
    n_head = devices.shape[0]
    fine = Mesh(devices.reshape((n_head,) + sizes), ("head",) + CTX)
    return jax.shard_map(
        make_local(sizes, n_head),
        mesh=fine,
        in_specs=(
            P("head", CTX),
            P("head", CTX),
            P(CTX, "head"),
            P(CTX, "head", None),
            P(CTX, None, None),
        ),
        out_specs=(P(CTX, "head"), P(CTX, "head"), P(CTX, "head")),
        check_vma=False,
    )
```

```python
import math

import jax
import jax.numpy as jnp
import numpy as np
from jax import lax
from jax.sharding import Mesh
from jax.sharding import PartitionSpec as P

HD = 128
CTX = ("x", "y", "core")
CHIPS = ("x", "y")

def unpack_bits(packed, heads_here):
    shifts = jnp.arange(16, dtype=jnp.int32).reshape(1, 1, 16, 1)
    spread = jnp.right_shift(packed.reshape(heads_here, -1, 1, packed.shape[-1]), shifts)
    return jnp.bitwise_and(spread, 1).astype(jnp.bfloat16).reshape(heads_here, -1, packed.shape[-1])


def token_mask(tiles, tile_size):
    tile_count = tiles.shape[0]
    tile_index = jnp.arange(tile_count, dtype=jnp.int32)
    lower = tile_index[:, None] > tile_index[None, :]
    diagonal = tile_index[:, None] == tile_index[None, :]
    allowed = jnp.where(diagonal, 1.0, jnp.where(lower, tiles.astype(jnp.float32), 0.0))
    span_width = tile_count * tile_size
    expanded = jnp.broadcast_to(
        allowed[:, None, :, None], (tile_count, tile_size, tile_count, tile_size)
    ).reshape(span_width, span_width)
    position = jnp.arange(span_width, dtype=jnp.int32)
    return jnp.where(position[:, None] >= position[None, :], expanded, 0.0)


def gather_heads(grad_out, n_head, width):
    tok_part = grad_out.shape[1]
    blocks = grad_out[0].reshape(tok_part, n_head, width).transpose(1, 0, 2)
    got = lax.all_to_all(blocks, "head", 0, 0, tiled=True)
    return got.reshape(n_head * tok_part, width)


def swap_core(a):
    return lax.ppermute(a, "core", [(0, 1), (1, 0)])


def carried_sums(state_term, adj_term, sizes):
    f32 = jnp.float32
    n_x, n_y, _ = sizes
    heads = state_term.shape[0]
    core = lax.axis_index("core")
    me_x = lax.axis_index("x")
    other_s = swap_core(state_term)
    other_a = swap_core(adj_term)
    chip = jnp.stack([state_term + other_s, adj_term + other_a]).reshape(2, n_y, -1, HD)
    mine = lax.dynamic_index_in_dim(chip, core, 0, keepdims=False)
    got = lax.all_to_all(mine, "y", 0, 0, tiled=True)
    row = jnp.arange(n_y, dtype=jnp.int32)[:, None]
    col = jnp.arange(n_y, dtype=jnp.int32)[None, :]
    mix = jnp.where(core == 0, col < row, col > row).astype(f32)
    flat = got.reshape(n_y, -1)
    in_row = jnp.dot(mix, flat, precision=lax.Precision.HIGHEST, preferred_element_type=f32)
    total = jnp.sum(got, axis=0)
    totals = lax.all_to_all(jnp.broadcast_to(total, (n_x,) + total.shape), "x", 0, 0, tiled=True)
    x_index = jnp.arange(n_x, dtype=jnp.int32)
    x_keep = jnp.where(core == 0, x_index < me_x, x_index > me_x)
    over_rows = jnp.sum(jnp.where(x_keep[:, None, None], totals, 0.0), axis=0)
    sums = in_row.reshape(got.shape) + over_rows[None]
    back = lax.all_to_all(sums, "y", 0, 0, tiled=True)
    mine_p = back.reshape(heads, HD, HD)
    other_p = swap_core(mine_p)
    state_p = jnp.where(core == 0, mine_p, other_p) + jnp.where(core == 1, other_s, 0.0)
    adj_p = jnp.where(core == 0, other_p, mine_p) + jnp.where(core == 0, other_a, 0.0)
    return state_p.astype(jnp.bfloat16), adj_p.astype(jnp.bfloat16)


def make_local(sizes, n_head):
    n_ctx = sizes[0] * sizes[1] * sizes[2]

    def local(query_bits, key_bits, values, grad_out, tile_mask):
        f32 = jnp.float32
        bf16 = jnp.bfloat16
        tok_rows = values.shape[0]
        head_group = values.shape[1] // HD
        att_scale = 4.0 / (HD * math.sqrt(tok_rows * n_ctx))
        q = unpack_bits(query_bits, head_group)
        k = unpack_bits(key_bits, head_group)
        v = values.reshape(tok_rows, head_group, HD)
        g = gather_heads(grad_out, n_head, values.shape[1]).reshape(tok_rows, head_group, HD)
        state_term = jnp.einsum("hds,she->hde", k, v, preferred_element_type=f32)
        adj_term = jnp.einsum("hdt,the->hde", q, g, preferred_element_type=f32)
        state, adjoint = carried_sums(state_term, adj_term, sizes)

        keep = token_mask(tile_mask[0], tok_rows // tile_mask.shape[1])
        pair = jnp.einsum("the,she->hts", g, v, preferred_element_type=f32)
        grad_w = (att_scale * pair * keep).astype(bf16)
        spk = jnp.einsum("hdt,hds->hts", q, k, preferred_element_type=f32)
        att_w = (att_scale * spk * keep).astype(bf16)
        query_grad = jnp.einsum("hts,hds->thd", grad_w, k, preferred_element_type=f32) + att_scale * jnp.einsum(
            "the,hde->thd", g, state, preferred_element_type=f32
        )
        key_grad = jnp.einsum("hts,hdt->shd", grad_w, q, preferred_element_type=f32) + att_scale * jnp.einsum(
            "she,hde->shd", v, adjoint, preferred_element_type=f32
        )
        value_grad = jnp.einsum("hts,the->she", att_w, g, preferred_element_type=f32) + att_scale * jnp.einsum(
            "hds,hde->she", k, adjoint, preferred_element_type=f32
        )
        shape = (tok_rows, head_group * HD)
        return (
            query_grad.astype(bf16).reshape(shape),
            key_grad.astype(bf16).reshape(shape),
            value_grad.astype(bf16).reshape(shape),
        )

    return local


def ctx_sizes(devices):
    n_ctx = devices.shape[1]
    n_core = 2
    try:
        n_y = len({d.coords[1] for d in devices[0]})
    except Exception:
        n_y = 8
    if n_y <= 0 or n_ctx % (n_core * n_y) != 0:
        n_y = 8
    return (n_ctx // (n_core * n_y), n_y, n_core)


def solution(mesh):
    devices = np.asarray(mesh.devices)
    sizes = ctx_sizes(devices)
    n_head = devices.shape[0]
    fine = Mesh(devices.reshape((n_head,) + sizes), ("head",) + CTX)
    return jax.shard_map(
        make_local(sizes, n_head),
        mesh=fine,
        in_specs=(
            P("head", CTX),
            P("head", CTX),
            P(CTX, "head"),
            P(CTX, "head", None),
            P(CTX, None, None),
        ),
        out_specs=(P(CTX, "head"), P(CTX, "head"), P(CTX, "head")),
        check_vma=False,
    )
```

```python
import math

import jax
import jax.numpy as jnp
import numpy as np
from jax import lax
from jax.sharding import Mesh
from jax.sharding import PartitionSpec as P

HD = 128
CTX = ("x", "y", "core")

def unpack_bits(packed, heads_here):
    shifts = jnp.arange(16, dtype=jnp.int32).reshape(1, 1, 16, 1)
    spread = jnp.right_shift(packed.reshape(heads_here, -1, 1, packed.shape[-1]), shifts)
    return jnp.bitwise_and(spread, 1).astype(jnp.bfloat16).reshape(heads_here, -1, packed.shape[-1])


def token_mask(tiles, tile_size):
    tile_count = tiles.shape[0]
    tile_index = jnp.arange(tile_count, dtype=jnp.int32)
    lower = tile_index[:, None] > tile_index[None, :]
    diagonal = tile_index[:, None] == tile_index[None, :]
    allowed = jnp.where(diagonal, 1.0, jnp.where(lower, tiles.astype(jnp.float32), 0.0))
    span_width = tile_count * tile_size
    expanded = jnp.broadcast_to(
        allowed[:, None, :, None], (tile_count, tile_size, tile_count, tile_size)
    ).reshape(span_width, span_width)
    position = jnp.arange(span_width, dtype=jnp.int32)
    return jnp.where(position[:, None] >= position[None, :], expanded, 0.0)


def gather_heads(grad_out, n_head, width):
    tok_part = grad_out.shape[1]
    blocks = grad_out[0].reshape(tok_part, n_head, width).transpose(1, 0, 2)
    got = lax.all_to_all(blocks, "head", 0, 0, tiled=True)
    return got.reshape(n_head * tok_part, width)


def carried_sums(state_term, adj_term, n_ctx):
    f32 = jnp.float32
    heads = state_term.shape[0]
    terms = jnp.concatenate([state_term, adj_term], axis=0).reshape(n_ctx, -1, HD)
    got = lax.all_to_all(terms, CTX, 0, 0, tiled=True)
    me = lax.axis_index(CTX)
    row = jnp.arange(n_ctx, dtype=jnp.int32)[:, None]
    col = jnp.arange(n_ctx, dtype=jnp.int32)[None, :]
    mix = jnp.where(me < n_ctx // 2, col < row, col > row).astype(f32)
    sums = jnp.dot(
        mix, got.reshape(n_ctx, -1), precision=lax.Precision.HIGHEST, preferred_element_type=f32
    )
    back = lax.all_to_all(sums.astype(jnp.bfloat16).reshape(n_ctx, -1, HD), CTX, 0, 0, tiled=True)
    both = back.reshape(2, heads, HD, HD)
    return both[0], both[1]


def make_local(sizes, n_head):
    n_ctx = sizes[0] * sizes[1] * sizes[2]

    def local(query_bits, key_bits, values, grad_out, tile_mask):
        f32 = jnp.float32
        bf16 = jnp.bfloat16
        tok_rows = values.shape[0]
        head_group = values.shape[1] // HD
        att_scale = 4.0 / (HD * math.sqrt(tok_rows * n_ctx))
        q = unpack_bits(query_bits, head_group)
        k = unpack_bits(key_bits, head_group)
        v = values.reshape(tok_rows, head_group, HD)
        g2 = gather_heads(grad_out, n_head, values.shape[1])
        g = g2.reshape(tok_rows, head_group, HD)
        state_term = jnp.einsum("hds,she->hde", k, v, preferred_element_type=f32)
        adj_term = jnp.einsum("hdt,the->hde", q, g, preferred_element_type=f32)
        state, adjoint = carried_sums(state_term, adj_term, n_ctx)

        keep = token_mask(tile_mask[0], tok_rows // tile_mask.shape[1])
        outs = ([], [], [])
        for h in range(head_group):
            cols = slice(h * HD, (h + 1) * HD)
            gh = g2[:, cols]
            vh = values[:, cols]
            qh = q[h]
            kh = k[h]
            pair = lax.dot_general(gh, vh, (((1,), (1,)), ((), ())), preferred_element_type=f32)
            grad_w = (att_scale * pair * keep).astype(bf16)
            spk = lax.dot_general(qh, kh, (((0,), (0,)), ((), ())), preferred_element_type=f32)
            att_w = (att_scale * spk * keep).astype(bf16)
            qg = lax.dot_general(grad_w, kh, (((1,), (1,)), ((), ())), preferred_element_type=f32)
            qg = qg + att_scale * lax.dot_general(gh, state[h], (((1,), (1,)), ((), ())), preferred_element_type=f32)
            kg = lax.dot_general(grad_w, qh, (((0,), (1,)), ((), ())), preferred_element_type=f32)
            kg = kg + att_scale * lax.dot_general(vh, adjoint[h], (((1,), (1,)), ((), ())), preferred_element_type=f32)
            vg = lax.dot_general(att_w, gh, (((0,), (0,)), ((), ())), preferred_element_type=f32)
            vg = vg + att_scale * lax.dot_general(kh, adjoint[h], (((0,), (0,)), ((), ())), preferred_element_type=f32)
            for out, part in zip(outs, (qg, kg, vg)):
                out.append(part.astype(bf16))
        return tuple(jnp.concatenate(out, axis=1) for out in outs)

    return local


def ctx_sizes(devices):
    n_ctx = devices.shape[1]
    n_core = 2
    try:
        n_y = len({d.coords[1] for d in devices[0]})
    except Exception:
        n_y = 8
    if n_y <= 0 or n_ctx % (n_core * n_y) != 0:
        n_y = 8
    return (n_ctx // (n_core * n_y), n_y, n_core)


def solution(mesh):
    devices = np.asarray(mesh.devices)
    sizes = ctx_sizes(devices)
    n_head = devices.shape[0]
    fine = Mesh(devices.reshape((n_head,) + sizes), ("head",) + CTX)
    return jax.shard_map(
        make_local(sizes, n_head),
        mesh=fine,
        in_specs=(
            P("head", CTX),
            P("head", CTX),
            P(CTX, "head"),
            P(CTX, "head", None),
            P(CTX, None, None),
        ),
        out_specs=(P(CTX, "head"), P(CTX, "head"), P(CTX, "head")),
        check_vma=False,
    )
```

```python
import math

import jax
import jax.numpy as jnp
import numpy as np
from jax import lax
from jax.experimental import pallas as pl
from jax.experimental.pallas import tpu as pltpu
from jax.sharding import Mesh
from jax.sharding import PartitionSpec as P

HD = 128
CTX = ("x", "y", "core")

def unpack_bits(packed, heads_here):
    shifts = jnp.arange(16, dtype=jnp.int32).reshape(1, 1, 16, 1)
    spread = jnp.right_shift(packed.reshape(heads_here, -1, 1, packed.shape[-1]), shifts)
    return jnp.bitwise_and(spread, 1).astype(jnp.bfloat16).reshape(heads_here, -1, packed.shape[-1])


def token_mask(tiles, tile_size):
    tile_count = tiles.shape[0]
    tile_index = jnp.arange(tile_count, dtype=jnp.int32)
    lower = tile_index[:, None] > tile_index[None, :]
    diagonal = tile_index[:, None] == tile_index[None, :]
    allowed = jnp.where(diagonal, 1.0, jnp.where(lower, tiles.astype(jnp.float32), 0.0))
    span_width = tile_count * tile_size
    expanded = jnp.broadcast_to(
        allowed[:, None, :, None], (tile_count, tile_size, tile_count, tile_size)
    ).reshape(span_width, span_width)
    position = jnp.arange(span_width, dtype=jnp.int32)
    return jnp.where(position[:, None] >= position[None, :], expanded, 0.0)


def gather_heads(grad_out, n_head, width):
    tok_part = grad_out.shape[1]
    blocks = grad_out[0].reshape(tok_part, n_head, width).transpose(1, 0, 2)
    got = lax.all_to_all(blocks, "head", 0, 0, tiled=True)
    return got.reshape(n_head * tok_part, width)


def carried_sums(state_term, adj_term, n_ctx):
    f32 = jnp.float32
    heads = state_term.shape[0]
    terms = jnp.concatenate([state_term, adj_term], axis=0).reshape(n_ctx, -1, HD)
    got = lax.all_to_all(terms, CTX, 0, 0, tiled=True)
    me = lax.axis_index(CTX)
    row = jnp.arange(n_ctx, dtype=jnp.int32)[:, None]
    col = jnp.arange(n_ctx, dtype=jnp.int32)[None, :]
    mix = jnp.where(me < n_ctx // 2, col < row, col > row).astype(f32)
    sums = jnp.dot(
        mix, got.reshape(n_ctx, -1), precision=lax.Precision.HIGHEST, preferred_element_type=f32
    )
    back = lax.all_to_all(sums.astype(jnp.bfloat16).reshape(n_ctx, -1, HD), CTX, 0, 0, tiled=True)
    both = back.reshape(2, heads, HD, HD)
    return both[0], both[1]


def finish_kernel(att_scale, intra_q, intra_k, intra_v, g, v, k_rows, state, adjoint, out_q, out_k, out_v):
    f32 = jnp.float32
    nt = (((1,), (1,)), ((), ()))
    nn = (((1,), (0,)), ((), ()))
    for h in range(state.shape[0]):
        cols = pl.ds(h * HD, HD)
        gh = g[:, cols]
        vh = v[:, cols]
        qg = lax.dot_general(gh, state[h], nt, preferred_element_type=f32)
        kg = lax.dot_general(vh, adjoint[h], nt, preferred_element_type=f32)
        vg = lax.dot_general(k_rows[h], adjoint[h], nn, preferred_element_type=f32)
        out_q[:, cols] = (intra_q[h] + att_scale * qg).astype(out_q.dtype)
        out_k[:, cols] = (intra_k[h] + att_scale * kg).astype(out_k.dtype)
        out_v[:, cols] = (intra_v[h] + att_scale * vg).astype(out_v.dtype)


def finish(att_scale, intra_q, intra_k, intra_v, g, v, k_rows, state, adjoint):
    heads, rows, _ = intra_q.shape
    shape = jax.ShapeDtypeStruct((rows, heads * HD), jnp.bfloat16)
    flops = 3 * 2 * heads * rows * HD * HD
    moved = 3 * heads * rows * HD * 4 + 3 * rows * heads * HD * 2 + 3 * rows * heads * HD * 2
    return pl.pallas_call(
        lambda *refs: finish_kernel(att_scale, *refs),
        out_shape=(shape, shape, shape),
        in_specs=[pl.BlockSpec(memory_space=pltpu.VMEM)] * 8,
        out_specs=[pl.BlockSpec(memory_space=pltpu.VMEM)] * 3,
        cost_estimate=pl.CostEstimate(flops=flops, bytes_accessed=moved, transcendentals=0),
        name="finish_outputs",
    )(intra_q, intra_k, intra_v, g, v, k_rows, state, adjoint)


def make_local(sizes, n_head):
    n_ctx = sizes[0] * sizes[1] * sizes[2]

    def local(query_bits, key_bits, values, grad_out, tile_mask):
        f32 = jnp.float32
        bf16 = jnp.bfloat16
        tok_rows = values.shape[0]
        head_group = values.shape[1] // HD
        att_scale = 4.0 / (HD * math.sqrt(tok_rows * n_ctx))
        q = unpack_bits(query_bits, head_group)
        k = unpack_bits(key_bits, head_group)
        v = values.reshape(tok_rows, head_group, HD)
        g2 = gather_heads(grad_out, n_head, values.shape[1])
        g = g2.reshape(tok_rows, head_group, HD)
        state_term = jnp.einsum("hds,she->hde", k, v, preferred_element_type=f32)
        adj_term = jnp.einsum("hdt,the->hde", q, g, preferred_element_type=f32)
        state, adjoint = carried_sums(state_term, adj_term, n_ctx)

        keep = token_mask(tile_mask[0], tok_rows // tile_mask.shape[1])
        pair = jnp.einsum("the,she->hts", g, v, preferred_element_type=f32)
        grad_w = (att_scale * pair * keep).astype(bf16)
        spk = jnp.einsum("hdt,hds->hts", q, k, preferred_element_type=f32)
        att_w = (att_scale * spk * keep).astype(bf16)
        intra_q = jnp.einsum("hts,hds->htd", grad_w, k, preferred_element_type=f32)
        intra_k = jnp.einsum("hts,hdt->hsd", grad_w, q, preferred_element_type=f32)
        intra_v = jnp.einsum("hts,the->hse", att_w, g, preferred_element_type=f32)
        k_rows = jnp.swapaxes(k, 1, 2)
        return finish(att_scale, intra_q, intra_k, intra_v, g2, values, k_rows, state, adjoint)

    return local


def ctx_sizes(devices):
    n_ctx = devices.shape[1]
    n_core = 2
    try:
        n_y = len({d.coords[1] for d in devices[0]})
    except Exception:
        n_y = 8
    if n_y <= 0 or n_ctx % (n_core * n_y) != 0:
        n_y = 8
    return (n_ctx // (n_core * n_y), n_y, n_core)


def solution(mesh):
    devices = np.asarray(mesh.devices)
    sizes = ctx_sizes(devices)
    n_head = devices.shape[0]
    fine = Mesh(devices.reshape((n_head,) + sizes), ("head",) + CTX)
    return jax.shard_map(
        make_local(sizes, n_head),
        mesh=fine,
        in_specs=(
            P("head", CTX),
            P("head", CTX),
            P(CTX, "head"),
            P(CTX, "head", None),
            P(CTX, None, None),
        ),
        out_specs=(P(CTX, "head"), P(CTX, "head"), P(CTX, "head")),
        check_vma=False,
    )
```

```python
import math

import jax
import jax.numpy as jnp
import numpy as np
from jax import lax
from jax.experimental import pallas as pl
from jax.experimental.pallas import tpu as pltpu
from jax.sharding import Mesh
from jax.sharding import PartitionSpec as P

HD = 128
CTX = ("x", "y", "core")

def unpack_bits(packed, heads_here):
    shifts = jnp.arange(16, dtype=jnp.int32).reshape(1, 1, 16, 1)
    spread = jnp.right_shift(packed.reshape(heads_here, -1, 1, packed.shape[-1]), shifts)
    return jnp.bitwise_and(spread, 1).astype(jnp.bfloat16).reshape(heads_here, -1, packed.shape[-1])


def token_mask(tiles, tile_size):
    tile_count = tiles.shape[0]
    tile_index = jnp.arange(tile_count, dtype=jnp.int32)
    lower = tile_index[:, None] > tile_index[None, :]
    diagonal = tile_index[:, None] == tile_index[None, :]
    allowed = jnp.where(diagonal, 1.0, jnp.where(lower, tiles.astype(jnp.float32), 0.0))
    span_width = tile_count * tile_size
    expanded = jnp.broadcast_to(
        allowed[:, None, :, None], (tile_count, tile_size, tile_count, tile_size)
    ).reshape(span_width, span_width)
    position = jnp.arange(span_width, dtype=jnp.int32)
    return jnp.where(position[:, None] >= position[None, :], expanded, 0.0)


def gather_heads(grad_out, n_head, width):
    tok_part = grad_out.shape[1]
    blocks = grad_out[0].reshape(tok_part, n_head, width)
    got = lax.all_to_all(blocks, "head", 1, 0, tiled=True)
    return got.reshape(n_head * tok_part, width)


def carried_sums(state_term, adj_term, n_ctx):
    f32 = jnp.float32
    heads = state_term.shape[0]
    terms = jnp.concatenate([state_term, adj_term], axis=0).reshape(n_ctx, -1, HD)
    got = lax.all_to_all(terms, CTX, 0, 0, tiled=True)
    me = lax.axis_index(CTX)
    row = jnp.arange(n_ctx, dtype=jnp.int32)[:, None]
    col = jnp.arange(n_ctx, dtype=jnp.int32)[None, :]
    mix = jnp.where(me < n_ctx // 2, col < row, col > row).astype(f32)
    sums = jnp.einsum(
        "ij,jrc->irc", mix, got, precision=lax.Precision.HIGHEST, preferred_element_type=f32
    )
    back = lax.all_to_all(sums.astype(jnp.bfloat16), CTX, 0, 0, tiled=True)
    return back.reshape(2, heads, HD, HD)


def finish_kernel(att_scale, intra_q, intra_k, intra_v, g, v, k_rows, carried, out_q, out_k, out_v):
    f32 = jnp.float32
    nt = (((1,), (1,)), ((), ()))
    nn = (((1,), (0,)), ((), ()))
    for h in range(carried.shape[1]):
        cols = pl.ds(h * HD, HD)
        gh = g[:, cols]
        vh = v[:, cols]
        qg = lax.dot_general(gh, carried[0, h], nt, preferred_element_type=f32)
        kg = lax.dot_general(vh, carried[1, h], nt, preferred_element_type=f32)
        vg = lax.dot_general(k_rows[h], carried[1, h], nn, preferred_element_type=f32)
        out_q[:, cols] = (intra_q[h] + att_scale * qg).astype(out_q.dtype)
        out_k[:, cols] = (intra_k[h] + att_scale * kg).astype(out_k.dtype)
        out_v[:, cols] = (intra_v[h] + att_scale * vg).astype(out_v.dtype)


def finish(att_scale, intra_q, intra_k, intra_v, g, v, k_rows, carried):
    heads, rows, _ = intra_q.shape
    shape = jax.ShapeDtypeStruct((rows, heads * HD), jnp.bfloat16)
    flops = 3 * 2 * heads * rows * HD * HD
    moved = 3 * heads * rows * HD * 4 + 3 * rows * heads * HD * 2 + 3 * rows * heads * HD * 2
    return pl.pallas_call(
        lambda *refs: finish_kernel(att_scale, *refs),
        out_shape=(shape, shape, shape),
        in_specs=[pl.BlockSpec(memory_space=pltpu.VMEM)] * 7,
        out_specs=[pl.BlockSpec(memory_space=pltpu.VMEM)] * 3,
        cost_estimate=pl.CostEstimate(flops=flops, bytes_accessed=moved, transcendentals=0),
        name="finish_outputs",
    )(intra_q, intra_k, intra_v, g, v, k_rows, carried)


def make_local(sizes, n_head):
    n_ctx = sizes[0] * sizes[1] * sizes[2]

    def local(query_bits, key_bits, values, grad_out, tile_mask):
        f32 = jnp.float32
        bf16 = jnp.bfloat16
        tok_rows = values.shape[0]
        head_group = values.shape[1] // HD
        att_scale = 4.0 / (HD * math.sqrt(tok_rows * n_ctx))
        q = unpack_bits(query_bits, head_group)
        k = unpack_bits(key_bits, head_group)
        v = values.reshape(tok_rows, head_group, HD)
        g2 = gather_heads(grad_out, n_head, values.shape[1])
        g = g2.reshape(tok_rows, head_group, HD)
        state_term = jnp.einsum("hds,she->hde", k, v, preferred_element_type=f32)
        adj_term = jnp.einsum("hdt,the->hde", q, g, preferred_element_type=f32)
        carried = carried_sums(state_term, adj_term, n_ctx)

        keep = token_mask(tile_mask[0], tok_rows // tile_mask.shape[1])
        pair = jnp.einsum("the,she->hts", g, v, preferred_element_type=f32)
        grad_w = (att_scale * pair * keep).astype(bf16)
        spk = jnp.einsum("hdt,hds->hts", q, k, preferred_element_type=f32)
        att_w = (att_scale * spk * keep).astype(bf16)
        intra_q = jnp.einsum("hts,hds->htd", grad_w, k, preferred_element_type=f32)
        intra_k = jnp.einsum("hts,hdt->hsd", grad_w, q, preferred_element_type=f32)
        intra_v = jnp.einsum("hts,the->hse", att_w, g, preferred_element_type=f32)
        k_rows = jnp.swapaxes(k, 1, 2)
        return finish(att_scale, intra_q, intra_k, intra_v, g2, values, k_rows, carried)

    return local


def ctx_sizes(devices):
    n_ctx = devices.shape[1]
    n_core = 2
    try:
        n_y = len({d.coords[1] for d in devices[0]})
    except Exception:
        n_y = 8
    if n_y <= 0 or n_ctx % (n_core * n_y) != 0:
        n_y = 8
    return (n_ctx // (n_core * n_y), n_y, n_core)


def solution(mesh):
    devices = np.asarray(mesh.devices)
    sizes = ctx_sizes(devices)
    n_head = devices.shape[0]
    fine = Mesh(devices.reshape((n_head,) + sizes), ("head",) + CTX)
    return jax.shard_map(
        make_local(sizes, n_head),
        mesh=fine,
        in_specs=(
            P("head", CTX),
            P("head", CTX),
            P(CTX, "head"),
            P(CTX, "head", None),
            P(CTX, None, None),
        ),
        out_specs=(P(CTX, "head"), P(CTX, "head"), P(CTX, "head")),
        check_vma=False,
    )
```

```python
import math

import jax
import jax.numpy as jnp
import numpy as np
from jax import lax
from jax.experimental import pallas as pl
from jax.experimental.pallas import tpu as pltpu
from jax.sharding import Mesh
from jax.sharding import PartitionSpec as P

HD = 128
CTX = ("x", "y", "core")

def unpack_bits(packed, heads_here):
    shifts = jnp.arange(16, dtype=jnp.int32).reshape(1, 1, 16, 1)
    spread = jnp.right_shift(packed.reshape(heads_here, -1, 1, packed.shape[-1]), shifts)
    return jnp.bitwise_and(spread, 1).astype(jnp.bfloat16).reshape(heads_here, -1, packed.shape[-1])


def token_mask(tiles, tile_size):
    tile_count = tiles.shape[0]
    tile_index = jnp.arange(tile_count, dtype=jnp.int32)
    lower = tile_index[:, None] > tile_index[None, :]
    diagonal = tile_index[:, None] == tile_index[None, :]
    allowed = jnp.where(diagonal, 1.0, jnp.where(lower, tiles.astype(jnp.float32), 0.0))
    span_width = tile_count * tile_size
    expanded = jnp.broadcast_to(
        allowed[:, None, :, None], (tile_count, tile_size, tile_count, tile_size)
    ).reshape(span_width, span_width)
    position = jnp.arange(span_width, dtype=jnp.int32)
    return jnp.where(position[:, None] >= position[None, :], expanded, 0.0)


def gather_heads(grad_out, n_head, width):
    tok_part = grad_out.shape[1]
    blocks = grad_out[0].reshape(tok_part, n_head, width)
    got = lax.all_to_all(blocks, "head", 1, 0, tiled=True)
    return got.reshape(n_head * tok_part, width)


def carried_sums(state_term, adj_term, n_ctx):
    f32 = jnp.float32
    heads = state_term.shape[0]
    terms = jnp.concatenate([state_term, adj_term], axis=0).reshape(n_ctx, -1, HD)
    got = lax.all_to_all(terms, CTX, 0, 0, tiled=True)
    me = lax.axis_index(CTX)
    row = jnp.arange(n_ctx, dtype=jnp.int32)[:, None]
    col = jnp.arange(n_ctx, dtype=jnp.int32)[None, :]
    mix = jnp.where(me < n_ctx // 2, col < row, col > row).astype(f32)
    sums = jnp.einsum(
        "ij,jrc->irc", mix, got, precision=lax.Precision.HIGHEST, preferred_element_type=f32
    )
    back = lax.all_to_all(sums.astype(jnp.bfloat16), CTX, 0, 0, tiled=True)
    return back.reshape(2, heads, HD, HD)


def finish_kernel(att_scale, intra_q, intra_k, intra_v, g, v, k_rows, carried, out_q, out_k, out_v):
    f32 = jnp.float32
    nt = (((1,), (1,)), ((), ()))
    nn = (((1,), (0,)), ((), ()))
    qg = lax.dot_general(g[...], carried[0, 0], nt, preferred_element_type=f32)
    kg = lax.dot_general(v[...], carried[1, 0], nt, preferred_element_type=f32)
    vg = lax.dot_general(k_rows[0], carried[1, 0], nn, preferred_element_type=f32)
    out_q[...] = (intra_q[0] + att_scale * qg).astype(out_q.dtype)
    out_k[...] = (intra_k[0] + att_scale * kg).astype(out_k.dtype)
    out_v[...] = (intra_v[0] + att_scale * vg).astype(out_v.dtype)


def finish(att_scale, intra_q, intra_k, intra_v, g, v, k_rows, carried):
    heads, rows, _ = intra_q.shape
    shape = jax.ShapeDtypeStruct((rows, heads * HD), jnp.bfloat16)
    flops = 3 * 2 * heads * rows * HD * HD
    moved = 3 * heads * rows * HD * 4 + 3 * rows * heads * HD * 2 + 3 * rows * heads * HD * 2
    per_head = pl.BlockSpec((1, rows, HD), lambda h: (h, 0, 0))
    columns = pl.BlockSpec((rows, HD), lambda h: (0, h))
    return pl.pallas_call(
        lambda *refs: finish_kernel(att_scale, *refs),
        out_shape=(shape, shape, shape),
        grid=(heads,),
        in_specs=[
            per_head,
            per_head,
            per_head,
            columns,
            columns,
            per_head,
            pl.BlockSpec((2, 1, HD, HD), lambda h: (0, h, 0, 0)),
        ],
        out_specs=[columns, columns, columns],
        cost_estimate=pl.CostEstimate(flops=flops, bytes_accessed=moved, transcendentals=0),
        name="finish_outputs",
    )(intra_q, intra_k, intra_v, g, v, k_rows, carried)


def make_local(sizes, n_head):
    n_ctx = sizes[0] * sizes[1] * sizes[2]

    def local(query_bits, key_bits, values, grad_out, tile_mask):
        f32 = jnp.float32
        bf16 = jnp.bfloat16
        tok_rows = values.shape[0]
        head_group = values.shape[1] // HD
        att_scale = 4.0 / (HD * math.sqrt(tok_rows * n_ctx))
        q = unpack_bits(query_bits, head_group)
        k = unpack_bits(key_bits, head_group)
        v = values.reshape(tok_rows, head_group, HD)
        g2 = gather_heads(grad_out, n_head, values.shape[1])
        g = g2.reshape(tok_rows, head_group, HD)
        state_term = jnp.einsum("hds,she->hde", k, v, preferred_element_type=f32)
        adj_term = jnp.einsum("hdt,the->hde", q, g, preferred_element_type=f32)
        carried = carried_sums(state_term, adj_term, n_ctx)

        keep = token_mask(tile_mask[0], tok_rows // tile_mask.shape[1])
        pair = jnp.einsum("the,she->hts", g, v, preferred_element_type=f32)
        grad_w = (att_scale * pair * keep).astype(bf16)
        spk = jnp.einsum("hdt,hds->hts", q, k, preferred_element_type=f32)
        att_w = (att_scale * spk * keep).astype(bf16)
        intra_q = jnp.einsum("hts,hds->htd", grad_w, k, preferred_element_type=f32)
        intra_k = jnp.einsum("hts,hdt->hsd", grad_w, q, preferred_element_type=f32)
        intra_v = jnp.einsum("hts,the->hse", att_w, g, preferred_element_type=f32)
        k_rows = jnp.swapaxes(k, 1, 2)
        return finish(att_scale, intra_q, intra_k, intra_v, g2, values, k_rows, carried)

    return local


def ctx_sizes(devices):
    n_ctx = devices.shape[1]
    n_core = 2
    try:
        n_y = len({d.coords[1] for d in devices[0]})
    except Exception:
        n_y = 8
    if n_y <= 0 or n_ctx % (n_core * n_y) != 0:
        n_y = 8
    return (n_ctx // (n_core * n_y), n_y, n_core)


def solution(mesh):
    devices = np.asarray(mesh.devices)
    sizes = ctx_sizes(devices)
    n_head = devices.shape[0]
    fine = Mesh(devices.reshape((n_head,) + sizes), ("head",) + CTX)
    return jax.shard_map(
        make_local(sizes, n_head),
        mesh=fine,
        in_specs=(
            P("head", CTX),
            P("head", CTX),
            P(CTX, "head"),
            P(CTX, "head", None),
            P(CTX, None, None),
        ),
        out_specs=(P(CTX, "head"), P(CTX, "head"), P(CTX, "head")),
        check_vma=False,
    )
```

```python
import math

import jax
import jax.numpy as jnp
import numpy as np
from jax import lax
from jax.experimental import pallas as pl
from jax.experimental.pallas import tpu as pltpu
from jax.sharding import Mesh
from jax.sharding import PartitionSpec as P

HD = 128
CTX = ("x", "y", "core")

def unpack_bits(packed, heads_here):
    shifts = jnp.arange(16, dtype=jnp.int32).reshape(1, 1, 16, 1)
    spread = jnp.right_shift(packed.reshape(heads_here, -1, 1, packed.shape[-1]), shifts)
    return jnp.bitwise_and(spread, 1).astype(jnp.bfloat16).reshape(heads_here, -1, packed.shape[-1])


def token_mask(tiles, tile_size):
    tile_count = tiles.shape[0]
    tile_index = jnp.arange(tile_count, dtype=jnp.int32)
    lower = tile_index[:, None] > tile_index[None, :]
    diagonal = tile_index[:, None] == tile_index[None, :]
    allowed = jnp.where(diagonal, 1.0, jnp.where(lower, tiles.astype(jnp.float32), 0.0))
    span_width = tile_count * tile_size
    expanded = jnp.broadcast_to(
        allowed[:, None, :, None], (tile_count, tile_size, tile_count, tile_size)
    ).reshape(span_width, span_width)
    position = jnp.arange(span_width, dtype=jnp.int32)
    return jnp.where(position[:, None] >= position[None, :], expanded, 0.0)


def gather_heads(grad_out, n_head, width):
    tok_part = grad_out.shape[1]
    blocks = grad_out[0].reshape(tok_part, n_head, width)
    got = lax.all_to_all(blocks, "head", 1, 0, tiled=True)
    return got.reshape(n_head * tok_part, width)


def running_kernel(flag, got, out):
    n = got.shape[0]
    reverse = flag[0]

    def step(i, acc):
        at = jnp.where(reverse == 1, n - 1 - i, i)
        out[at] = acc.astype(out.dtype)
        return acc + got[at]

    lax.fori_loop(0, n, step, jnp.zeros(got.shape[1:], jnp.float32), unroll=8)


def running_sums(flag, got):
    return pl.pallas_call(
        running_kernel,
        out_shape=jax.ShapeDtypeStruct(got.shape, jnp.bfloat16),
        in_specs=[pl.BlockSpec(memory_space=pltpu.SMEM), pl.BlockSpec(memory_space=pltpu.VMEM)],
        out_specs=pl.BlockSpec(memory_space=pltpu.VMEM),
        name="running_sums",
    )(flag, got)


def carried_sums(state_term, adj_term, n_ctx):
    heads = state_term.shape[0]
    terms = jnp.concatenate([state_term, adj_term], axis=0).reshape(n_ctx, -1, HD)
    got = lax.all_to_all(terms, CTX, 0, 0, tiled=True)
    me = lax.axis_index(CTX)
    flag = jnp.where(me < n_ctx // 2, 0, 1).astype(jnp.int32).reshape(1)
    back = lax.all_to_all(running_sums(flag, got), CTX, 0, 0, tiled=True)
    return back.reshape(2, heads, HD, HD)


def finish_kernel(att_scale, intra_q, intra_k, intra_v, g, v, k_rows, carried, out_q, out_k, out_v):
    f32 = jnp.float32
    nt = (((1,), (1,)), ((), ()))
    nn = (((1,), (0,)), ((), ()))
    for h in range(carried.shape[1]):
        cols = pl.ds(h * HD, HD)
        gh = g[:, cols]
        vh = v[:, cols]
        qg = lax.dot_general(gh, carried[0, h], nt, preferred_element_type=f32)
        kg = lax.dot_general(vh, carried[1, h], nt, preferred_element_type=f32)
        vg = lax.dot_general(k_rows[h], carried[1, h], nn, preferred_element_type=f32)
        out_q[:, cols] = (intra_q[h] + att_scale * qg).astype(out_q.dtype)
        out_k[:, cols] = (intra_k[h] + att_scale * kg).astype(out_k.dtype)
        out_v[:, cols] = (intra_v[h] + att_scale * vg).astype(out_v.dtype)


def finish(att_scale, intra_q, intra_k, intra_v, g, v, k_rows, carried):
    heads, rows, _ = intra_q.shape
    shape = jax.ShapeDtypeStruct((rows, heads * HD), jnp.bfloat16)
    flops = 3 * 2 * heads * rows * HD * HD
    moved = 3 * heads * rows * HD * 4 + 3 * rows * heads * HD * 2 + 3 * rows * heads * HD * 2
    return pl.pallas_call(
        lambda *refs: finish_kernel(att_scale, *refs),
        out_shape=(shape, shape, shape),
        in_specs=[pl.BlockSpec(memory_space=pltpu.VMEM)] * 7,
        out_specs=[pl.BlockSpec(memory_space=pltpu.VMEM)] * 3,
        cost_estimate=pl.CostEstimate(flops=flops, bytes_accessed=moved, transcendentals=0),
        name="finish_outputs",
    )(intra_q, intra_k, intra_v, g, v, k_rows, carried)


def make_local(sizes, n_head):
    n_ctx = sizes[0] * sizes[1] * sizes[2]

    def local(query_bits, key_bits, values, grad_out, tile_mask):
        f32 = jnp.float32
        bf16 = jnp.bfloat16
        tok_rows = values.shape[0]
        head_group = values.shape[1] // HD
        att_scale = 4.0 / (HD * math.sqrt(tok_rows * n_ctx))
        q = unpack_bits(query_bits, head_group)
        k = unpack_bits(key_bits, head_group)
        v = values.reshape(tok_rows, head_group, HD)
        g2 = gather_heads(grad_out, n_head, values.shape[1])
        g = g2.reshape(tok_rows, head_group, HD)
        state_term = jnp.einsum("hds,she->hde", k, v, preferred_element_type=f32)
        adj_term = jnp.einsum("hdt,the->hde", q, g, preferred_element_type=f32)
        carried = carried_sums(state_term, adj_term, n_ctx)

        keep = token_mask(tile_mask[0], tok_rows // tile_mask.shape[1])
        pair = jnp.einsum("the,she->hts", g, v, preferred_element_type=f32)
        grad_w = (att_scale * pair * keep).astype(bf16)
        spk = jnp.einsum("hdt,hds->hts", q, k, preferred_element_type=f32)
        att_w = (att_scale * spk * keep).astype(bf16)
        intra_q = jnp.einsum("hts,hds->htd", grad_w, k, preferred_element_type=f32)
        intra_k = jnp.einsum("hts,hdt->hsd", grad_w, q, preferred_element_type=f32)
        intra_v = jnp.einsum("hts,the->hse", att_w, g, preferred_element_type=f32)
        k_rows = jnp.swapaxes(k, 1, 2)
        return finish(att_scale, intra_q, intra_k, intra_v, g2, values, k_rows, carried)

    return local


def ctx_sizes(devices):
    n_ctx = devices.shape[1]
    n_core = 2
    try:
        n_y = len({d.coords[1] for d in devices[0]})
    except Exception:
        n_y = 8
    if n_y <= 0 or n_ctx % (n_core * n_y) != 0:
        n_y = 8
    return (n_ctx // (n_core * n_y), n_y, n_core)


def solution(mesh):
    devices = np.asarray(mesh.devices)
    sizes = ctx_sizes(devices)
    n_head = devices.shape[0]
    fine = Mesh(devices.reshape((n_head,) + sizes), ("head",) + CTX)
    return jax.shard_map(
        make_local(sizes, n_head),
        mesh=fine,
        in_specs=(
            P("head", CTX),
            P("head", CTX),
            P(CTX, "head"),
            P(CTX, "head", None),
            P(CTX, None, None),
        ),
        out_specs=(P(CTX, "head"), P(CTX, "head"), P(CTX, "head")),
        check_vma=False,
    )
```

```python
import math

import jax
import jax.numpy as jnp
import numpy as np
from jax import lax
from jax.sharding import Mesh
from jax.sharding import PartitionSpec as P

HD = 128
CTX = ("x", "y", "core")

def unpack_bits(packed, heads_here):
    shifts = jnp.arange(16, dtype=jnp.int32).reshape(1, 1, 16, 1)
    spread = jnp.right_shift(packed.reshape(heads_here, -1, 1, packed.shape[-1]), shifts)
    return jnp.bitwise_and(spread, 1).astype(jnp.bfloat16).reshape(heads_here, -1, packed.shape[-1])


def token_mask(tiles, tile_size):
    tile_count = tiles.shape[0]
    tile_index = jnp.arange(tile_count, dtype=jnp.int32)
    lower = tile_index[:, None] > tile_index[None, :]
    diagonal = tile_index[:, None] == tile_index[None, :]
    allowed = jnp.where(diagonal, 1.0, jnp.where(lower, tiles.astype(jnp.float32), 0.0))
    span_width = tile_count * tile_size
    expanded = jnp.broadcast_to(
        allowed[:, None, :, None], (tile_count, tile_size, tile_count, tile_size)
    ).reshape(span_width, span_width)
    position = jnp.arange(span_width, dtype=jnp.int32)
    return jnp.where(position[:, None] >= position[None, :], expanded, 0.0)


def gather_heads(grad_out, n_head, width):
    tok_part = grad_out.shape[1]
    blocks = jnp.concatenate(
        [grad_out[0, :, j * width : (j + 1) * width] for j in range(n_head)], axis=0
    ).reshape(n_head, tok_part, width)
    got = lax.all_to_all(blocks, "head", 0, 0, tiled=True)
    return got.reshape(n_head * tok_part, width)


def carried_sums(state_term, adj_term, n_ctx):
    f32 = jnp.float32
    heads = state_term.shape[0]
    terms = jnp.concatenate([state_term, adj_term], axis=0).reshape(n_ctx, -1, HD)
    got = lax.all_to_all(terms, CTX, 0, 0, tiled=True)
    me = lax.axis_index(CTX)
    row = jnp.arange(n_ctx, dtype=jnp.int32)[:, None]
    col = jnp.arange(n_ctx, dtype=jnp.int32)[None, :]
    mix = jnp.where(me < n_ctx // 2, col < row, col > row).astype(f32)
    sums = jnp.dot(
        mix, got.reshape(n_ctx, -1), precision=lax.Precision.HIGHEST, preferred_element_type=f32
    )
    back = lax.all_to_all(sums.astype(jnp.bfloat16).reshape(n_ctx, -1, HD), CTX, 0, 0, tiled=True)
    both = back.reshape(2, heads, HD, HD)
    return both[0], both[1]


def make_local(sizes, n_head):
    n_ctx = sizes[0] * sizes[1] * sizes[2]

    def local(query_bits, key_bits, values, grad_out, tile_mask):
        f32 = jnp.float32
        bf16 = jnp.bfloat16
        tok_rows = values.shape[0]
        head_group = values.shape[1] // HD
        att_scale = 4.0 / (HD * math.sqrt(tok_rows * n_ctx))
        q = unpack_bits(query_bits, head_group)
        k = unpack_bits(key_bits, head_group)
        v = values.reshape(tok_rows, head_group, HD)
        g = gather_heads(grad_out, n_head, values.shape[1]).reshape(tok_rows, head_group, HD)
        state_term = jnp.einsum("hds,she->hde", k, v, preferred_element_type=f32)
        adj_term = jnp.einsum("hdt,the->hde", q, g, preferred_element_type=f32)
        state, adjoint = carried_sums(state_term, adj_term, n_ctx)

        keep = token_mask(tile_mask[0], tok_rows // tile_mask.shape[1])
        pair = jnp.einsum("the,she->hts", g, v, preferred_element_type=f32)
        grad_w = (att_scale * pair * keep).astype(bf16)
        spk = jnp.einsum("hdt,hds->hts", q, k, preferred_element_type=f32)
        att_w = (att_scale * spk * keep).astype(bf16)
        query_grad = jnp.einsum("hts,hds->thd", grad_w, k, preferred_element_type=f32) + att_scale * jnp.einsum(
            "the,hde->thd", g, state, preferred_element_type=f32
        )
        key_grad = jnp.einsum("hts,hdt->shd", grad_w, q, preferred_element_type=f32) + att_scale * jnp.einsum(
            "she,hde->shd", v, adjoint, preferred_element_type=f32
        )
        value_grad = jnp.einsum("hts,the->she", att_w, g, preferred_element_type=f32) + att_scale * jnp.einsum(
            "hds,hde->she", k, adjoint, preferred_element_type=f32
        )
        shape = (tok_rows, head_group * HD)
        return (
            query_grad.astype(bf16).reshape(shape),
            key_grad.astype(bf16).reshape(shape),
            value_grad.astype(bf16).reshape(shape),
        )

    return local


def ctx_sizes(devices):
    n_ctx = devices.shape[1]
    n_core = 2
    try:
        n_y = len({d.coords[1] for d in devices[0]})
    except Exception:
        n_y = 8
    if n_y <= 0 or n_ctx % (n_core * n_y) != 0:
        n_y = 8
    return (n_ctx // (n_core * n_y), n_y, n_core)


def solution(mesh):
    devices = np.asarray(mesh.devices)
    sizes = ctx_sizes(devices)
    n_head = devices.shape[0]
    fine = Mesh(devices.reshape((n_head,) + sizes), ("head",) + CTX)
    return jax.shard_map(
        make_local(sizes, n_head),
        mesh=fine,
        in_specs=(
            P("head", CTX),
            P("head", CTX),
            P(CTX, "head"),
            P(CTX, "head", None),
            P(CTX, None, None),
        ),
        out_specs=(P(CTX, "head"), P(CTX, "head"), P(CTX, "head")),
        check_vma=False,
    )
```

```python
import math

import jax
import jax.numpy as jnp
import numpy as np
from jax import lax
from jax.experimental import pallas as pl
from jax.experimental.pallas import tpu as pltpu
from jax.sharding import Mesh
from jax.sharding import PartitionSpec as P

HD = 128
CTX = ("x", "y", "core")

def unpack_bits(packed, heads_here):
    shifts = jnp.arange(16, dtype=jnp.int32).reshape(1, 1, 16, 1)
    spread = jnp.right_shift(packed.reshape(heads_here, -1, 1, packed.shape[-1]), shifts)
    return jnp.bitwise_and(spread, 1).astype(jnp.bfloat16).reshape(heads_here, -1, packed.shape[-1])


def token_mask(tiles, tile_size):
    tile_count = tiles.shape[0]
    tile_index = jnp.arange(tile_count, dtype=jnp.int32)
    lower = tile_index[:, None] > tile_index[None, :]
    diagonal = tile_index[:, None] == tile_index[None, :]
    allowed = jnp.where(diagonal, 1.0, jnp.where(lower, tiles.astype(jnp.float32), 0.0))
    span_width = tile_count * tile_size
    expanded = jnp.broadcast_to(
        allowed[:, None, :, None], (tile_count, tile_size, tile_count, tile_size)
    ).reshape(span_width, span_width)
    position = jnp.arange(span_width, dtype=jnp.int32)
    return jnp.where(position[:, None] >= position[None, :], expanded, 0.0)


def gather_heads(grad_out, n_head, width):
    tok_part = grad_out.shape[1]
    blocks = grad_out[0].reshape(tok_part, n_head, width)
    got = lax.all_to_all(blocks, "head", 1, 0, tiled=True)
    return got.reshape(n_head * tok_part, width)


def carried_sums(state_term, adj_term, n_ctx):
    f32 = jnp.float32
    heads = state_term.shape[0]
    terms = jnp.concatenate([state_term, adj_term], axis=0).reshape(n_ctx, -1, HD)
    got = lax.all_to_all(terms, CTX, 0, 0, tiled=True)
    me = lax.axis_index(CTX)
    row = jnp.arange(n_ctx, dtype=jnp.int32)[:, None]
    col = jnp.arange(n_ctx, dtype=jnp.int32)[None, :]
    mix = jnp.where(me < n_ctx // 2, col < row, col > row).astype(f32)
    sums = jnp.einsum(
        "ij,jrc->irc", mix, got, precision=lax.Precision.HIGHEST, preferred_element_type=f32
    )
    back = lax.all_to_all(sums.astype(jnp.bfloat16), CTX, 0, 0, tiled=True)
    return back.reshape(2, heads, HD, HD)


def finish_kernel(att_scale, intra_q, intra_k, intra_v, g, v, k_rows, carried, out_q, out_k, out_v):
    f32 = jnp.float32
    nt = (((1,), (1,)), ((), ()))
    nn = (((1,), (0,)), ((), ()))
    for h in range(carried.shape[1]):
        cols = pl.ds(h * HD, HD)
        gh = g[:, cols]
        vh = v[:, cols]
        qg = lax.dot_general(gh, carried[0, h], nt, preferred_element_type=f32)
        kg = lax.dot_general(vh, carried[1, h], nt, preferred_element_type=f32)
        vg = lax.dot_general(k_rows[h], carried[1, h], nn, preferred_element_type=f32)
        out_q[:, cols] = (intra_q[h].astype(f32) + att_scale * qg).astype(out_q.dtype)
        out_k[:, cols] = (intra_k[h].astype(f32) + att_scale * kg).astype(out_k.dtype)
        out_v[:, cols] = (intra_v[h].astype(f32) + att_scale * vg).astype(out_v.dtype)


def finish(att_scale, intra_q, intra_k, intra_v, g, v, k_rows, carried):
    heads, rows, _ = intra_q.shape
    shape = jax.ShapeDtypeStruct((rows, heads * HD), jnp.bfloat16)
    flops = 3 * 2 * heads * rows * HD * HD
    moved = 3 * heads * rows * HD * 2 + 3 * rows * heads * HD * 2 + 3 * rows * heads * HD * 2
    return pl.pallas_call(
        lambda *refs: finish_kernel(att_scale, *refs),
        out_shape=(shape, shape, shape),
        in_specs=[pl.BlockSpec(memory_space=pltpu.VMEM)] * 7,
        out_specs=[pl.BlockSpec(memory_space=pltpu.VMEM)] * 3,
        cost_estimate=pl.CostEstimate(flops=flops, bytes_accessed=moved, transcendentals=0),
        name="finish_outputs",
    )(intra_q, intra_k, intra_v, g, v, k_rows, carried)


def make_local(sizes, n_head):
    n_ctx = sizes[0] * sizes[1] * sizes[2]

    def local(query_bits, key_bits, values, grad_out, tile_mask):
        f32 = jnp.float32
        bf16 = jnp.bfloat16
        tok_rows = values.shape[0]
        head_group = values.shape[1] // HD
        att_scale = 4.0 / (HD * math.sqrt(tok_rows * n_ctx))
        q = unpack_bits(query_bits, head_group)
        k = unpack_bits(key_bits, head_group)
        v = values.reshape(tok_rows, head_group, HD)
        g2 = gather_heads(grad_out, n_head, values.shape[1])
        g = g2.reshape(tok_rows, head_group, HD)
        state_term = jnp.einsum("hds,she->hde", k, v, preferred_element_type=f32)
        adj_term = jnp.einsum("hdt,the->hde", q, g, preferred_element_type=f32)
        carried = carried_sums(state_term, adj_term, n_ctx)

        keep = token_mask(tile_mask[0], tok_rows // tile_mask.shape[1])
        pair = jnp.einsum("the,she->hts", g, v, preferred_element_type=f32)
        grad_w = (att_scale * pair * keep).astype(bf16)
        spk = jnp.einsum("hdt,hds->hts", q, k, preferred_element_type=f32)
        att_w = (att_scale * spk * keep).astype(bf16)
        intra_q = jnp.einsum("hts,hds->htd", grad_w, k, preferred_element_type=f32)
        intra_k = jnp.einsum("hts,hdt->hsd", grad_w, q, preferred_element_type=f32)
        intra_v = jnp.einsum("hts,the->hse", att_w, g, preferred_element_type=f32)
        k_rows = jnp.swapaxes(k, 1, 2)
        return finish(
            att_scale,
            intra_q.astype(bf16),
            intra_k.astype(bf16),
            intra_v.astype(bf16),
            g2,
            values,
            k_rows,
            carried,
        )

    return local


def ctx_sizes(devices):
    n_ctx = devices.shape[1]
    n_core = 2
    try:
        n_y = len({d.coords[1] for d in devices[0]})
    except Exception:
        n_y = 8
    if n_y <= 0 or n_ctx % (n_core * n_y) != 0:
        n_y = 8
    return (n_ctx // (n_core * n_y), n_y, n_core)


def solution(mesh):
    devices = np.asarray(mesh.devices)
    sizes = ctx_sizes(devices)
    n_head = devices.shape[0]
    fine = Mesh(devices.reshape((n_head,) + sizes), ("head",) + CTX)
    return jax.shard_map(
        make_local(sizes, n_head),
        mesh=fine,
        in_specs=(
            P("head", CTX),
            P("head", CTX),
            P(CTX, "head"),
            P(CTX, "head", None),
            P(CTX, None, None),
        ),
        out_specs=(P(CTX, "head"), P(CTX, "head"), P(CTX, "head")),
        check_vma=False,
    )
```

```python
import math

import jax
import jax.numpy as jnp
import numpy as np
from jax import lax
from jax.sharding import Mesh
from jax.sharding import PartitionSpec as P

HD = 128
CTX = ("x", "y", "core")

def unpack_bits(packed, heads_here):
    shifts = jnp.arange(16, dtype=jnp.int32).reshape(1, 1, 16, 1)
    spread = jnp.right_shift(packed.reshape(heads_here, -1, 1, packed.shape[-1]), shifts)
    return jnp.bitwise_and(spread, 1).astype(jnp.bfloat16).reshape(heads_here, -1, packed.shape[-1])


def token_mask(tiles, tile_size):
    tile_count = tiles.shape[0]
    tile_index = jnp.arange(tile_count, dtype=jnp.int32)
    lower = tile_index[:, None] > tile_index[None, :]
    diagonal = tile_index[:, None] == tile_index[None, :]
    allowed = jnp.where(diagonal, 1.0, jnp.where(lower, tiles.astype(jnp.float32), 0.0))
    span_width = tile_count * tile_size
    expanded = jnp.broadcast_to(
        allowed[:, None, :, None], (tile_count, tile_size, tile_count, tile_size)
    ).reshape(span_width, span_width)
    position = jnp.arange(span_width, dtype=jnp.int32)
    return jnp.where(position[:, None] >= position[None, :], expanded, 0.0)


def gather_heads(grad_out, n_head, width):
    tok_part = grad_out.shape[1]
    blocks = grad_out[0].reshape(tok_part, n_head, width).transpose(1, 0, 2)
    got = lax.all_to_all(blocks, "head", 0, 0, tiled=True)
    return got.reshape(n_head * tok_part, width)


def carried_sums(state_term, adj_term, n_ctx):
    f32 = jnp.float32
    heads = state_term.shape[0]
    terms = jnp.concatenate([state_term, adj_term], axis=0).reshape(n_ctx, -1, HD)
    got = lax.all_to_all(terms, CTX, 0, 0, tiled=True)
    me = lax.axis_index(CTX)
    row = jnp.arange(n_ctx, dtype=jnp.int32)[:, None]
    col = jnp.arange(n_ctx, dtype=jnp.int32)[None, :]
    mix = jnp.where(me < n_ctx // 2, col < row, col > row).astype(f32)
    sums = jnp.dot(
        mix, got.reshape(n_ctx, -1), precision=lax.Precision.HIGH, preferred_element_type=f32
    )
    back = lax.all_to_all(sums.astype(jnp.bfloat16).reshape(n_ctx, -1, HD), CTX, 0, 0, tiled=True)
    both = back.reshape(2, heads, HD, HD)
    return both[0], both[1]


def make_local(sizes, n_head):
    n_ctx = sizes[0] * sizes[1] * sizes[2]

    def local(query_bits, key_bits, values, grad_out, tile_mask):
        f32 = jnp.float32
        bf16 = jnp.bfloat16
        tok_rows = values.shape[0]
        head_group = values.shape[1] // HD
        att_scale = 4.0 / (HD * math.sqrt(tok_rows * n_ctx))
        q = unpack_bits(query_bits, head_group)
        k = unpack_bits(key_bits, head_group)
        v = values.reshape(tok_rows, head_group, HD)
        g = gather_heads(grad_out, n_head, values.shape[1]).reshape(tok_rows, head_group, HD)
        state_term = jnp.einsum("hds,she->hde", k, v, preferred_element_type=f32)
        adj_term = jnp.einsum("hdt,the->hde", q, g, preferred_element_type=f32)
        state, adjoint = carried_sums(state_term, adj_term, n_ctx)

        keep = token_mask(tile_mask[0], tok_rows // tile_mask.shape[1])
        pair = jnp.einsum("the,she->hts", g, v, preferred_element_type=f32)
        grad_w = (att_scale * pair * keep).astype(bf16)
        spk = jnp.einsum("hdt,hds->hts", q, k, preferred_element_type=f32)
        att_w = (att_scale * spk * keep).astype(bf16)
        query_grad = jnp.einsum("hts,hds->thd", grad_w, k, preferred_element_type=f32) + att_scale * jnp.einsum(
            "the,hde->thd", g, state, preferred_element_type=f32
        )
        key_grad = jnp.einsum("hts,hdt->shd", grad_w, q, preferred_element_type=f32) + att_scale * jnp.einsum(
            "she,hde->shd", v, adjoint, preferred_element_type=f32
        )
        value_grad = jnp.einsum("hts,the->she", att_w, g, preferred_element_type=f32) + att_scale * jnp.einsum(
            "hds,hde->she", k, adjoint, preferred_element_type=f32
        )
        shape = (tok_rows, head_group * HD)
        return (
            query_grad.astype(bf16).reshape(shape),
            key_grad.astype(bf16).reshape(shape),
            value_grad.astype(bf16).reshape(shape),
        )

    return local


def ctx_sizes(devices):
    n_ctx = devices.shape[1]
    n_core = 2
    try:
        n_y = len({d.coords[1] for d in devices[0]})
    except Exception:
        n_y = 8
    if n_y <= 0 or n_ctx % (n_core * n_y) != 0:
        n_y = 8
    return (n_ctx // (n_core * n_y), n_y, n_core)


def solution(mesh):
    devices = np.asarray(mesh.devices)
    sizes = ctx_sizes(devices)
    n_head = devices.shape[0]
    fine = Mesh(devices.reshape((n_head,) + sizes), ("head",) + CTX)
    return jax.shard_map(
        make_local(sizes, n_head),
        mesh=fine,
        in_specs=(
            P("head", CTX),
            P("head", CTX),
            P(CTX, "head"),
            P(CTX, "head", None),
            P(CTX, None, None),
        ),
        out_specs=(P(CTX, "head"), P(CTX, "head"), P(CTX, "head")),
        check_vma=False,
    )
```
